512 devices in a mesh: head: 8 (over x, core), expert: 64 (over z, y).
Axes of the slice: x: 4, y: 4, z: 16, core: 2. Of those that a mesh axis runs over, the one named last changes fastest.
Arguments:
- q_latent: bfloat16 [512, 64, 512], P('expert', 'head'), may hold values from -16 to 16
- q_rotary: bfloat16 [512, 64, 64], P('expert', 'head'), may hold values from -3 to 3
- cache_latent: bfloat16 [512, 128, 512], P('expert'), may hold values from -5 to 5
- cache_rotary: bfloat16 [512, 64, 128], P('expert'), may hold values from -5 to 5
- lengths: int32 [512], P('expert'), may hold values from 16 to 128, as said below
- w_value_out: bfloat16 [32768, 5120], P('head', 'expert'), may hold values from -0.25 to 0.25
- resid: bfloat16 [512, 5120], P('expert'), may hold values from -8 to 8
- norm_gain: float32 [5120], replicated, may hold values from 0.1 to 1.9
- route_ids: int32 [512, 6], P('expert'), may hold values from 0 to 63, as said below
- route_weights: float32 [512, 6], P('expert'), may hold values from 0.1 to 0.6
- w_gate_up: bfloat16 [64, 2, 768, 5120], P('expert', None, 'head'), may hold values from -0.078125 to 0.078125
- w_down: bfloat16 [64, 768, 5120], P('expert', 'head'), may hold values from -0.21875 to 0.21875
Outputs:
- mixed_out: float32 [512, 5120], P('expert', 'head')
The draws below stay inside these ranges and needn't reach their ends.
Inputs may be any that keep to these rules, and one draw needn't show every extreme that they name: `lengths`: slots at positions below a sequence's length are valid; some sequence has length 128. `route_ids`: each row names 6 different experts. Among the rows of one device (aligned blocks of 8 rows) no expert is named by more than 2 rows, and one expert is named by exactly 2 rows in every block.
All inputs are finite; a program needn't handle non-finite values.
Results may differ from the reference program's by a relative error of at most 0.0046.
Values may be sent and summed in bfloat16 or wider, within the bound.
No kernel may reach another device: no remote copies, remote signals or barrier semaphores. Data moves between devices by JAX's collectives and lax.ppermute only.
A program may use at most 64 MiB of HBM per device.

```python
import jax
import jax.numpy as jnp
from jax import lax

D = 5120
HEADS = 64
LAT = 512
ROPE = 64
FF = 768
TOPK = 6
CAP = 128
SEQ_DEV = 8
SEQS = 512
EXPERTS = 64
MOST = 2
N_EXPERT = 64


def attention_fields(key):
    query_lat = jnp.clip(jax.random.normal(jax.random.fold_in(key, 11), (SEQS, HEADS, LAT)) * 0.6, -3.0, 3.0)
    query_rot = jnp.clip(jax.random.normal(jax.random.fold_in(key, 12), (SEQS, HEADS, ROPE)) * 0.6, -3.0, 3.0)
    cache_lat = jnp.clip(jax.random.normal(jax.random.fold_in(key, 13), (SEQS, CAP, LAT)), -5.0, 5.0)
    cache_rot = jnp.clip(jax.random.normal(jax.random.fold_in(key, 14), (SEQS, ROPE, CAP)), -5.0, 5.0)
    return (query_lat, query_rot, cache_lat, cache_rot)


def draw_q_latent(key, part):
    return attention_fields(key)[0].astype(jnp.bfloat16)


def draw_q_rotary(key, part):
    return attention_fields(key)[1].astype(jnp.bfloat16)


def draw_cache_latent(key, part):
    return attention_fields(key)[2].astype(jnp.bfloat16)


def draw_cache_rotary(key, part):
    return attention_fields(key)[3].astype(jnp.bfloat16)


def draw_lengths(key, part):
    drawn = jax.random.randint(jax.random.fold_in(key, 31), (SEQS,), CAP // 8, CAP + 1)
    longest = jax.random.randint(jax.random.fold_in(key, 32), (), 0, SEQS)
    return jnp.where(jnp.arange(SEQS) == longest, CAP, drawn).astype(jnp.int32)


def draw_resid(key, part):
    values = jnp.clip(jax.random.normal(jax.random.fold_in(key, 41), (SEQS, D)), -6.0, 6.0)
    return values.astype(jnp.bfloat16)


def draw_route_ids(key, part):
    block_count = SEQS // SEQ_DEV
    assigned = SEQ_DEV * TOPK
    span_size = (assigned + MOST - 1) // MOST
    popularity = jax.random.randint(jax.random.fold_in(key, 21), (EXPERTS,), 0, 4)
    hottest = jax.random.randint(jax.random.fold_in(key, 22), (), 0, EXPERTS)
    jitter = jax.random.randint(jax.random.fold_in(key, 23), (block_count, EXPERTS), 0, 1024)
    expert_ids = jnp.arange(EXPERTS, dtype=jnp.int32)
    ranking_score = jitter + popularity[None, :] * 256 + jnp.where(expert_ids == hottest, 1 << 20, 0)[None, :]
    distinct = ranking_score * EXPERTS + expert_ids[None, :]
    ranking = jnp.argsort(-distinct, axis=1)
    positions = jnp.arange(assigned, dtype=jnp.int32) % span_size
    picked = jnp.take(ranking, positions, axis=1)
    return picked.reshape(SEQS, TOPK).astype(jnp.int32)


def levels(key, dims, cuts, low, top_value):
    factor_of, own = 1.0, jax.random.fold_in(key, 6)
    for dim, parts in cuts:
        heights = jnp.exp(jax.random.uniform(jax.random.fold_in(own, dim), (parts,), jnp.float32, low / len(cuts), top_value / len(cuts)))
        factor_of = factor_of * jnp.repeat(heights, dims[dim] // parts).reshape([-1 if axis == dim else 1 for axis in range(len(dims))])
    return factor_of


def normal_values(key, extent, width, bound, shards=(), kind=jnp.bfloat16):
    entries = width * jax.random.normal(key, extent, jnp.float32)
    if shards:
        entries = entries * levels(key, extent, shards, -0.22, 0.18)
    return jnp.clip(entries, -bound, bound).astype(kind)


def setup_inputs(seed: int = 0) -> dict:
    splits = jax.random.split(jax.random.key(seed), 13)
    return {
        "q_latent": draw_q_latent(jax.random.fold_in(splits[12], 71), 0),
        "q_rotary": draw_q_rotary(jax.random.fold_in(splits[12], 71), 0),
        "cache_latent": draw_cache_latent(jax.random.fold_in(splits[12], 71), 0),
        "cache_rotary": draw_cache_rotary(jax.random.fold_in(splits[12], 71), 0),
        "lengths": draw_lengths(jax.random.fold_in(splits[12], 71), 0),
        "w_value_out": normal_values(splits[5], (HEADS * LAT, D), LAT ** -0.5, 0.25, ((0, 8), (1, 64))),
        "resid": draw_resid(jax.random.fold_in(splits[12], 71), 0),
        "norm_gain": jnp.clip(1.0 + 0.18 * jax.random.normal(splits[7], (D,), jnp.float32), 0.1, 1.9),
        "route_ids": draw_route_ids(jax.random.fold_in(splits[12], 71), 0),
        "route_weights": jnp.clip(0.1 + 0.5 * jax.random.uniform(splits[9], (SEQS, TOPK), jnp.float32) ** levels(splits[9], (SEQS, TOPK), ((0, 64),), -0.2, 0.2), 0.1, 0.6),
        "w_gate_up": normal_values(splits[10], (EXPERTS, 2, FF, D), D ** -0.5, 0.078125, ((0, 64), (2, 8))),
        "w_down": normal_values(splits[11], (EXPERTS, FF, D), FF ** -0.5, 0.21875, ((0, 64), (1, 8))),
    }


softmax_scale = 192.0 ** (-0.5)
norm_epsilon = 1e-06

def reference(q_latent, q_rotary, cache_latent, cache_rotary, lengths, w_value_out, resid, norm_gain, route_ids, route_weights, w_gate_up, w_down):
    cache_float = cache_latent.astype(jnp.float32)
    scores = jnp.einsum('shl,scl->shc', q_latent.astype(jnp.float32), cache_float)
    scores = scores + jnp.einsum('shr,src->shc', q_rotary.astype(jnp.float32), cache_rotary.astype(jnp.float32))
    scores = scores * softmax_scale
    position = jnp.arange(CAP, dtype=jnp.int32)
    valid_slot = position[None, None, :] < lengths[:, None, None]
    scores = jnp.where(valid_slot, scores, -1e+30)
    highest = lax.optimization_barrier(jnp.max(scores, axis=2, keepdims=True))
    weights = jnp.exp(scores - highest)
    probs = (weights / lax.optimization_barrier(jnp.sum(weights, axis=2, keepdims=True))).astype(jnp.bfloat16)
    latent_out = jnp.einsum('shc,scl->shl', probs.astype(jnp.float32), cache_float).astype(jnp.bfloat16)
    flattened = latent_out.reshape(SEQS, HEADS * LAT)
    attention = jnp.dot(flattened, w_value_out, preferred_element_type=jnp.float32).astype(jnp.bfloat16)
    stream = resid.astype(jnp.float32) + attention.astype(jnp.float32)
    mean_square = lax.optimization_barrier(jnp.mean(stream * stream, axis=1, keepdims=True))
    normed = (stream * lax.rsqrt(mean_square + norm_epsilon) * norm_gain).astype(jnp.bfloat16)
    flat_ids = route_ids.reshape(-1)
    flat_weights = route_weights.reshape(-1)
    token_of = jnp.arange(SEQS * TOPK, dtype=jnp.int32) // TOPK
    limit = N_EXPERT * MOST

    def add_expert(total, item):
        index, gate_up, down_matrix = item
        chosen = flat_ids == index
        picks = jnp.nonzero(chosen, size=limit, fill_value=0)[0].astype(jnp.int32)
        valid_row = jnp.arange(limit, dtype=jnp.int32) < jnp.sum(chosen.astype(jnp.int32))
        token_rows = token_of[picks]
        inputs = normed[token_rows]
        projected = jnp.einsum('rd,gfd->rgf', inputs.astype(jnp.float32), gate_up.astype(jnp.float32))
        hidden = (jax.nn.silu(projected[:, 0]) * projected[:, 1]).astype(jnp.bfloat16)
        expert_out = jnp.dot(hidden, down_matrix, preferred_element_type=jnp.float32).astype(jnp.bfloat16)
        row_weight = jnp.where(valid_row, flat_weights[picks], 0.0)
        total = total.at[token_rows].add(expert_out.astype(jnp.float32) * row_weight[:, None])
        return (total, None)
    mixture, unused = lax.scan(add_expert, jnp.zeros((SEQS, D), jnp.float32), (jnp.arange(EXPERTS, dtype=jnp.int32), w_gate_up, w_down))
    return stream + mixture
```

```python
import jax
import jax.numpy as jnp
from jax import lax
from jax.sharding import PartitionSpec as P

softmax_scale = 192.0 ** (-0.5)
norm_epsilon = 1e-06


def attend(q_latent, q_rotary, cache_latent, cache_rotary, lengths):
    scores = jnp.einsum("shl,scl->shc", q_latent, cache_latent, preferred_element_type=jnp.float32)
    scores = scores + jnp.einsum(
        "shr,src->shc", q_rotary, cache_rotary, preferred_element_type=jnp.float32
    )
    scores = scores * softmax_scale
    position = lax.broadcasted_iota(jnp.int32, scores.shape, 2)
    scores = jnp.where(position < lengths[:, None, None], scores, -1e30)
    highest = jnp.max(scores, axis=2, keepdims=True)
    weights = jnp.exp(scores - highest)
    probs = (weights / jnp.sum(weights, axis=2, keepdims=True)).astype(jnp.bfloat16)
    return jnp.einsum(
        "shc,scl->shl", probs, cache_latent, preferred_element_type=jnp.float32
    ).astype(jnp.bfloat16)


def on_device(
    q_latent,
    q_rotary,
    cache_latent,
    cache_rotary,
    lengths,
    w_value_out,
    resid,
    norm_gain,
    route_ids,
    route_weights,
    w_gate_up,
    w_down,
):
    seq_local = q_latent.shape[0]
    latent_out = attend(q_latent, q_rotary, cache_latent, cache_rotary, lengths)
    flattened = latent_out.reshape(seq_local, -1)
    column_terms = jnp.dot(
        lax.all_gather(flattened, "expert", axis=0, tiled=True),
        w_value_out,
        preferred_element_type=jnp.float32,
    )
    column_sums = lax.psum(column_terms, "head")
    attention = lax.all_to_all(
        column_sums.astype(jnp.bfloat16), "expert", split_axis=0, concat_axis=1, tiled=True
    )
    stream = resid.astype(jnp.float32) + attention.astype(jnp.float32)
    mean_square = jnp.mean(stream * stream, axis=1, keepdims=True)
    normed = (stream * lax.rsqrt(mean_square + norm_epsilon) * norm_gain).astype(jnp.bfloat16)
    expert_count = lax.axis_size("expert")
    top_count = route_ids.shape[1]
    capacity = max(2, -(-(seq_local * top_count) // expert_count))
    flat_ids = route_ids.reshape(-1)
    one_hot = (flat_ids[:, None] == jnp.arange(expert_count, dtype=jnp.int32)[None, :]).astype(
        jnp.int32
    )
    earlier = jnp.cumsum(one_hot, axis=0) - one_hot
    slot_index = jnp.sum(earlier * one_hot, axis=1)
    target = (flat_ids * capacity + slot_index).reshape(seq_local, top_count)
    places = jnp.arange(expert_count * capacity, dtype=jnp.int32)
    matches = target[None, :, :] == places[:, None, None]
    selector = jnp.sum(matches.astype(jnp.int32), axis=2).astype(jnp.bfloat16)
    blending = jnp.sum(jnp.where(matches, route_weights[None, :, :], 0.0), axis=2)
    gate_up = w_gate_up[0]
    down_local = w_down[0]
    col_width = stream.shape[1] // lax.axis_size("head")
    offset = lax.axis_index("head") * col_width
    normed_cols = lax.dynamic_slice_in_dim(normed, offset, col_width, 1)
    outgoing = jnp.dot(selector, normed_cols, preferred_element_type=jnp.float32).astype(jnp.bfloat16)
    outgoing = outgoing.reshape(expert_count, capacity, -1)
    arrived = lax.all_to_all(outgoing, "expert", split_axis=0, concat_axis=0, tiled=True)
    arrived_cols = arrived.reshape(-1, arrived.shape[2])
    flat_rows = lax.all_gather(arrived_cols, "head", axis=1, tiled=True)
    projected = jnp.einsum("rd,gfd->rgf", flat_rows, gate_up, preferred_element_type=jnp.float32)
    hidden = (jax.nn.silu(projected[:, 0]) * projected[:, 1]).astype(jnp.bfloat16)
    partial_rows = jnp.dot(hidden, down_local, preferred_element_type=jnp.float32)
    summed_cols = lax.psum_scatter(
        partial_rows.astype(jnp.bfloat16), "head", scatter_dimension=1, tiled=True
    )
    summed_rows = summed_cols.reshape(expert_count, capacity, -1)
    returned = lax.all_to_all(summed_rows, "expert", split_axis=0, concat_axis=0, tiled=True)
    back_rows = returned.reshape(expert_count * capacity, -1).astype(jnp.float32)
    mixture = jnp.dot(blending.T, back_rows, precision=lax.Precision.HIGHEST)
    stream_cols = lax.dynamic_slice_in_dim(stream, offset, col_width, 1)
    return stream_cols + mixture


def solution(mesh):
    placed = (
        P("expert", "head", None),
        P("expert", "head", None),
        P("expert", None, None),
        P("expert", None, None),
        P("expert"),
        P("head", "expert"),
        P("expert", None),
        P(),
        P("expert", None),
        P("expert", None),
        P("expert", None, "head", None),
        P("expert", "head", None),
    )
    return jax.shard_map(
        on_device, mesh=mesh, in_specs=placed, out_specs=P("expert", "head"), check_vma=False
    )
```

```python
import jax
import jax.numpy as jnp
from jax import lax
from jax.sharding import Mesh
from jax.sharding import PartitionSpec as P

EXPERT = ("ez", "ey")
softmax_scale = 192.0 ** (-0.5)
norm_epsilon = 1e-06


def attend(q_latent, q_rotary, cache_latent, cache_rotary, lengths):
    scores = jnp.einsum("shl,scl->shc", q_latent, cache_latent, preferred_element_type=jnp.float32)
    scores = scores + jnp.einsum(
        "shr,src->shc", q_rotary, cache_rotary, preferred_element_type=jnp.float32
    )
    scores = scores * softmax_scale
    position = lax.broadcasted_iota(jnp.int32, scores.shape, 2)
    scores = jnp.where(position < lengths[:, None, None], scores, -1e30)
    highest = jnp.max(scores, axis=2, keepdims=True)
    weights = jnp.exp(scores - highest)
    probs = (weights / jnp.sum(weights, axis=2, keepdims=True)).astype(jnp.bfloat16)
    return jnp.einsum(
        "shc,scl->shl", probs, cache_latent, preferred_element_type=jnp.float32
    ).astype(jnp.bfloat16)


def on_device(
    q_latent,
    q_rotary,
    cache_latent,
    cache_rotary,
    lengths,
    w_value_out,
    resid,
    norm_gain,
    route_ids,
    route_weights,
    w_gate_up,
    w_down,
):
    seq_local = q_latent.shape[0]
    latent_out = attend(q_latent, q_rotary, cache_latent, cache_rotary, lengths)
    flattened = latent_out.reshape(seq_local, -1)
    gathered = lax.all_gather(flattened, "ey", axis=0, tiled=True)
    gathered = lax.all_gather(gathered, "ez", axis=0, tiled=True)
    column_terms = jnp.dot(
        gathered,
        w_value_out,
        preferred_element_type=jnp.float32,
    )
    column_sums = lax.psum(column_terms, "head")
    attention = lax.all_to_all(
        column_sums.astype(jnp.bfloat16), EXPERT, split_axis=0, concat_axis=1, tiled=True
    )
    stream = resid.astype(jnp.float32) + attention.astype(jnp.float32)
    mean_square = jnp.mean(stream * stream, axis=1, keepdims=True)
    normed = (stream * lax.rsqrt(mean_square + norm_epsilon) * norm_gain).astype(jnp.bfloat16)
    expert_count = lax.axis_size("ez") * lax.axis_size("ey")
    top_count = route_ids.shape[1]
    capacity = max(2, -(-(seq_local * top_count) // expert_count))
    flat_ids = route_ids.reshape(-1)
    one_hot = (flat_ids[:, None] == jnp.arange(expert_count, dtype=jnp.int32)[None, :]).astype(
        jnp.int32
    )
    earlier = jnp.cumsum(one_hot, axis=0) - one_hot
    slot_index = jnp.sum(earlier * one_hot, axis=1)
    target = (flat_ids * capacity + slot_index).reshape(seq_local, top_count)
    places = jnp.arange(expert_count * capacity, dtype=jnp.int32)
    matches = target[None, :, :] == places[:, None, None]
    selector = jnp.sum(matches.astype(jnp.int32), axis=2).astype(jnp.bfloat16)
    blending = jnp.sum(jnp.where(matches, route_weights[None, :, :], 0.0), axis=2)
    gate_up = w_gate_up[0]
    down_local = w_down[0]
    col_width = stream.shape[1] // lax.axis_size("head")
    offset = lax.axis_index("head") * col_width
    normed_cols = lax.dynamic_slice_in_dim(normed, offset, col_width, 1)
    outgoing = jnp.dot(selector, normed_cols, preferred_element_type=jnp.float32).astype(jnp.bfloat16)
    outgoing = outgoing.reshape(expert_count, capacity, -1)
    arrived = lax.all_to_all(outgoing, EXPERT, split_axis=0, concat_axis=0, tiled=True)
    arrived_cols = arrived.reshape(-1, arrived.shape[2])
    flat_rows = lax.all_gather(arrived_cols, "head", axis=1, tiled=True)
    projected = jnp.einsum("rd,gfd->rgf", flat_rows, gate_up, preferred_element_type=jnp.float32)
    hidden = (jax.nn.silu(projected[:, 0]) * projected[:, 1]).astype(jnp.bfloat16)
    partial_rows = jnp.dot(hidden, down_local, preferred_element_type=jnp.float32)
    summed_cols = lax.psum_scatter(
        partial_rows.astype(jnp.bfloat16), "head", scatter_dimension=1, tiled=True
    )
    summed_rows = summed_cols.reshape(expert_count, capacity, -1)
    returned = lax.all_to_all(summed_rows, EXPERT, split_axis=0, concat_axis=0, tiled=True)
    back_rows = returned.reshape(expert_count * capacity, -1).astype(jnp.float32)
    mixture = jnp.dot(blending.T, back_rows, precision=lax.Precision.HIGHEST)
    stream_cols = lax.dynamic_slice_in_dim(stream, offset, col_width, 1)
    return stream_cols + mixture


def solution(mesh):
    placed = (
        P(EXPERT, "head", None),
        P(EXPERT, "head", None),
        P(EXPERT, None, None),
        P(EXPERT, None, None),
        P(EXPERT),
        P("head", EXPERT),
        P(EXPERT, None),
        P(),
        P(EXPERT, None),
        P(EXPERT, None),
        P(EXPERT, None, "head", None),
        P(EXPERT, "head", None),
    )
    head_count, expert_total = mesh.devices.shape
    y_count = len({device.coords[1] for device in mesh.devices[0]})
    split_mesh = Mesh(
        mesh.devices.reshape(head_count, expert_total // y_count, y_count), ("head",) + EXPERT
    )
    return jax.shard_map(
        on_device, mesh=split_mesh, in_specs=placed, out_specs=P(EXPERT, "head"), check_vma=False
    )
```

```python
import jax
import jax.numpy as jnp
from jax import lax
from jax.sharding import Mesh
from jax.sharding import PartitionSpec as P

EXPERT = ("ez", "ey")
softmax_scale = 192.0 ** (-0.5)
norm_epsilon = 1e-06


def attend(q_latent, q_rotary, cache_latent, cache_rotary, lengths):
    scores = jnp.einsum("shl,scl->shc", q_latent, cache_latent, preferred_element_type=jnp.float32)
    scores = scores + jnp.einsum(
        "shr,src->shc", q_rotary, cache_rotary, preferred_element_type=jnp.float32
    )
    scores = scores * softmax_scale
    position = lax.broadcasted_iota(jnp.int32, scores.shape, 2)
    scores = jnp.where(position < lengths[:, None, None], scores, -1e30)
    highest = jnp.max(scores, axis=2, keepdims=True)
    weights = jnp.exp(scores - highest)
    probs = (weights / jnp.sum(weights, axis=2, keepdims=True)).astype(jnp.bfloat16)
    return jnp.einsum(
        "shc,scl->shl", probs, cache_latent, preferred_element_type=jnp.float32
    ).astype(jnp.bfloat16)


def on_device(
    q_latent,
    q_rotary,
    cache_latent,
    cache_rotary,
    lengths,
    w_value_out,
    resid,
    norm_gain,
    route_ids,
    route_weights,
    w_gate_up,
    w_down,
):
    seq_local = q_latent.shape[0]
    latent_out = attend(q_latent, q_rotary, cache_latent, cache_rotary, lengths)
    flattened = latent_out.reshape(seq_local, -1)
    gathered = lax.all_gather(flattened, "ez", axis=0, tiled=True)
    value_cols = lax.all_gather(w_value_out, "ey", axis=1, tiled=True)
    column_terms = jnp.dot(gathered, value_cols, preferred_element_type=jnp.float32)
    column_sums = lax.psum(column_terms, "head")
    attention = lax.all_to_all(
        column_sums.astype(jnp.bfloat16), "ez", split_axis=0, concat_axis=1, tiled=True
    )
    stream = resid.astype(jnp.float32) + attention.astype(jnp.float32)
    mean_square = jnp.mean(stream * stream, axis=1, keepdims=True)
    normed = (stream * lax.rsqrt(mean_square + norm_epsilon) * norm_gain).astype(jnp.bfloat16)
    expert_count = lax.axis_size("ez") * lax.axis_size("ey")
    top_count = route_ids.shape[1]
    capacity = max(2, -(-(seq_local * top_count) // expert_count))
    flat_ids = route_ids.reshape(-1)
    one_hot = (flat_ids[:, None] == jnp.arange(expert_count, dtype=jnp.int32)[None, :]).astype(
        jnp.int32
    )
    earlier = jnp.cumsum(one_hot, axis=0) - one_hot
    slot_index = jnp.sum(earlier * one_hot, axis=1)
    target = (flat_ids * capacity + slot_index).reshape(seq_local, top_count)
    places = jnp.arange(expert_count * capacity, dtype=jnp.int32)
    matches = target[None, :, :] == places[:, None, None]
    selector = jnp.sum(matches.astype(jnp.int32), axis=2).astype(jnp.bfloat16)
    blending = jnp.sum(jnp.where(matches, route_weights[None, :, :], 0.0), axis=2)
    gate_up = w_gate_up[0]
    down_local = w_down[0]
    col_width = stream.shape[1] // lax.axis_size("head")
    offset = lax.axis_index("head") * col_width
    normed_cols = lax.dynamic_slice_in_dim(normed, offset, col_width, 1)
    outgoing = jnp.dot(selector, normed_cols, preferred_element_type=jnp.float32).astype(jnp.bfloat16)
    outgoing = outgoing.reshape(expert_count, capacity, -1)
    arrived = lax.all_to_all(outgoing, EXPERT, split_axis=0, concat_axis=0, tiled=True)
    arrived_cols = arrived.reshape(-1, arrived.shape[2])
    flat_rows = lax.all_gather(arrived_cols, "head", axis=1, tiled=True)
    projected = jnp.einsum("rd,gfd->rgf", flat_rows, gate_up, preferred_element_type=jnp.float32)
    hidden = (jax.nn.silu(projected[:, 0]) * projected[:, 1]).astype(jnp.bfloat16)
    partial_rows = jnp.dot(hidden, down_local, preferred_element_type=jnp.float32)
    summed_cols = lax.psum_scatter(
        partial_rows.astype(jnp.bfloat16), "head", scatter_dimension=1, tiled=True
    )
    summed_rows = summed_cols.reshape(expert_count, capacity, -1)
    returned = lax.all_to_all(summed_rows, EXPERT, split_axis=0, concat_axis=0, tiled=True)
    back_rows = returned.reshape(expert_count * capacity, -1).astype(jnp.float32)
    mixture = jnp.dot(blending.T, back_rows, precision=lax.Precision.HIGHEST)
    stream_cols = lax.dynamic_slice_in_dim(stream, offset, col_width, 1)
    return stream_cols + mixture


def solution(mesh):
    placed = (
        P(EXPERT, "head", None),
        P(EXPERT, "head", None),
        P(EXPERT, None, None),
        P(EXPERT, None, None),
        P(EXPERT),
        P("head", EXPERT),
        P(EXPERT, None),
        P(),
        P(EXPERT, None),
        P(EXPERT, None),
        P(EXPERT, None, "head", None),
        P(EXPERT, "head", None),
    )
    head_count, expert_total = mesh.devices.shape
    y_count = len({device.coords[1] for device in mesh.devices[0]})
    split_mesh = Mesh(
        mesh.devices.reshape(head_count, expert_total // y_count, y_count), ("head",) + EXPERT
    )
    return jax.shard_map(
        on_device, mesh=split_mesh, in_specs=placed, out_specs=P(EXPERT, "head"), check_vma=False
    )
```

```python
import jax
import jax.numpy as jnp
from jax import lax
from jax.sharding import Mesh
from jax.sharding import PartitionSpec as P

EXPERT = ("ez", "ey")
softmax_scale = 192.0 ** (-0.5)
norm_epsilon = 1e-06


def attend(q_latent, q_rotary, cache_latent, cache_rotary, lengths):
    scores = jnp.einsum("shl,scl->shc", q_latent, cache_latent, preferred_element_type=jnp.float32)
    scores = scores + jnp.einsum(
        "shr,src->shc", q_rotary, cache_rotary, preferred_element_type=jnp.float32
    )
    scores = scores * softmax_scale
    position = lax.broadcasted_iota(jnp.int32, scores.shape, 2)
    scores = jnp.where(position < lengths[:, None, None], scores, -1e30)
    highest = jnp.max(scores, axis=2, keepdims=True)
    weights = jnp.exp(scores - highest)
    probs = (weights / jnp.sum(weights, axis=2, keepdims=True)).astype(jnp.bfloat16)
    return jnp.einsum(
        "shc,scl->shl", probs, cache_latent, preferred_element_type=jnp.float32
    ).astype(jnp.bfloat16)


def on_device(
    q_latent,
    q_rotary,
    cache_latent,
    cache_rotary,
    lengths,
    w_value_out,
    resid,
    norm_gain,
    route_ids,
    route_weights,
    w_gate_up,
    w_down,
):
    seq_local = q_latent.shape[0]
    latent_out = attend(q_latent, q_rotary, cache_latent, cache_rotary, lengths)
    flattened = latent_out.reshape(seq_local, -1)
    gathered = lax.all_gather(flattened, "ey", axis=0, tiled=True)
    gathered = lax.all_gather(gathered, "ez", axis=0, tiled=True)
    head_count = lax.axis_size("head")
    down_blocks = w_down[0].reshape(w_down.shape[1], head_count, -1)
    down_cols = lax.all_to_all(down_blocks, "head", split_axis=1, concat_axis=0, tiled=True)
    down_cols = down_cols.reshape(-1, down_blocks.shape[2])
    gathered, down_cols = lax.optimization_barrier((gathered, down_cols))
    column_terms = jnp.dot(
        gathered,
        w_value_out,
        preferred_element_type=jnp.float32,
    )
    column_sums = lax.psum(column_terms, "head")
    attention = lax.all_to_all(
        column_sums.astype(jnp.bfloat16), EXPERT, split_axis=0, concat_axis=1, tiled=True
    )
    stream = resid.astype(jnp.float32) + attention.astype(jnp.float32)
    mean_square = jnp.mean(stream * stream, axis=1, keepdims=True)
    normed = (stream * lax.rsqrt(mean_square + norm_epsilon) * norm_gain).astype(jnp.bfloat16)
    expert_count = lax.axis_size("ez") * lax.axis_size("ey")
    top_count = route_ids.shape[1]
    capacity = max(2, -(-(seq_local * top_count) // expert_count))
    flat_ids = route_ids.reshape(-1)
    one_hot = (flat_ids[:, None] == jnp.arange(expert_count, dtype=jnp.int32)[None, :]).astype(
        jnp.int32
    )
    earlier = jnp.cumsum(one_hot, axis=0) - one_hot
    slot_index = jnp.sum(earlier * one_hot, axis=1)
    target = (flat_ids * capacity + slot_index).reshape(seq_local, top_count)
    places = jnp.arange(expert_count * capacity, dtype=jnp.int32)
    matches = target[None, :, :] == places[:, None, None]
    selector = jnp.sum(matches.astype(jnp.int32), axis=2).astype(jnp.bfloat16)
    blending = jnp.sum(jnp.where(matches, route_weights[None, :, :], 0.0), axis=2)
    gate_up = w_gate_up[0]
    col_width = stream.shape[1] // lax.axis_size("head")
    offset = lax.axis_index("head") * col_width
    normed_cols = lax.dynamic_slice_in_dim(normed, offset, col_width, 1)
    outgoing = jnp.dot(selector, normed_cols, preferred_element_type=jnp.float32).astype(jnp.bfloat16)
    outgoing = outgoing.reshape(expert_count, capacity, -1)
    arrived = lax.all_to_all(outgoing, EXPERT, split_axis=0, concat_axis=0, tiled=True)
    arrived_cols = arrived.reshape(-1, arrived.shape[2])
    flat_rows = lax.all_gather(arrived_cols, "head", axis=1, tiled=True)
    projected = jnp.einsum("rd,gfd->rgf", flat_rows, gate_up, preferred_element_type=jnp.float32)
    hidden = (jax.nn.silu(projected[:, 0]) * projected[:, 1]).astype(jnp.bfloat16)
    hidden_all = lax.all_gather(hidden, "head", axis=1, tiled=True)
    summed_cols = jnp.dot(hidden_all, down_cols, preferred_element_type=jnp.float32).astype(jnp.bfloat16)
    summed_rows = summed_cols.reshape(expert_count, capacity, -1)
    returned = lax.all_to_all(summed_rows, EXPERT, split_axis=0, concat_axis=0, tiled=True)
    back_rows = returned.reshape(expert_count * capacity, -1).astype(jnp.float32)
    mixture = jnp.dot(blending.T, back_rows, precision=lax.Precision.HIGHEST)
    stream_cols = lax.dynamic_slice_in_dim(stream, offset, col_width, 1)
    return stream_cols + mixture


def solution(mesh):
    placed = (
        P(EXPERT, "head", None),
        P(EXPERT, "head", None),
        P(EXPERT, None, None),
        P(EXPERT, None, None),
        P(EXPERT),
        P("head", EXPERT),
        P(EXPERT, None),
        P(),
        P(EXPERT, None),
        P(EXPERT, None),
        P(EXPERT, None, "head", None),
        P(EXPERT, "head", None),
    )
    head_count, expert_total = mesh.devices.shape
    y_count = len({device.coords[1] for device in mesh.devices[0]})
    split_mesh = Mesh(
        mesh.devices.reshape(head_count, expert_total // y_count, y_count), ("head",) + EXPERT
    )
    return jax.shard_map(
        on_device, mesh=split_mesh, in_specs=placed, out_specs=P(EXPERT, "head"), check_vma=False
    )
```

```python
import jax
import jax.numpy as jnp
from jax import lax
from jax.sharding import Mesh
from jax.sharding import PartitionSpec as P

EXPERT = ("ez", "ey")
softmax_scale = 192.0 ** (-0.5)
norm_epsilon = 1e-06


def attend(q_latent, q_rotary, cache_latent, cache_rotary, lengths):
    scores = jnp.einsum("shl,scl->shc", q_latent, cache_latent, preferred_element_type=jnp.float32)
    scores = scores + jnp.einsum(
        "shr,src->shc", q_rotary, cache_rotary, preferred_element_type=jnp.float32
    )
    scores = scores * softmax_scale
    position = lax.broadcasted_iota(jnp.int32, scores.shape, 2)
    scores = jnp.where(position < lengths[:, None, None], scores, -1e30)
    highest = jnp.max(scores, axis=2, keepdims=True)
    weights = jnp.exp(scores - highest)
    probs = (weights / jnp.sum(weights, axis=2, keepdims=True)).astype(jnp.bfloat16)
    return jnp.einsum(
        "shc,scl->shl", probs, cache_latent, preferred_element_type=jnp.float32
    ).astype(jnp.bfloat16)


def on_device(
    q_latent,
    q_rotary,
    cache_latent,
    cache_rotary,
    lengths,
    w_value_out,
    resid,
    norm_gain,
    route_ids,
    route_weights,
    w_gate_up,
    w_down,
):
    seq_local = q_latent.shape[0]
    latent_out = attend(q_latent, q_rotary, cache_latent, cache_rotary, lengths)
    flattened = latent_out.reshape(seq_local, -1)
    gathered = lax.all_gather(flattened, "ez", axis=0, tiled=True)
    y_count = lax.axis_size("ey")
    value_copies = jnp.broadcast_to(w_value_out[None], (y_count,) + w_value_out.shape)
    value_blocks = lax.all_to_all(value_copies, "ey", split_axis=0, concat_axis=0, tiled=True)
    head_count = lax.axis_size("head")
    down_blocks = w_down[0].reshape(w_down.shape[1], head_count, -1)
    down_cols = lax.all_to_all(down_blocks, "head", split_axis=1, concat_axis=0, tiled=True)
    down_cols = down_cols.reshape(-1, down_blocks.shape[2])
    gathered, value_blocks, down_cols = lax.optimization_barrier((gathered, value_blocks, down_cols))
    column_terms = jnp.einsum(
        "sk,jkc->sjc", gathered, value_blocks, preferred_element_type=jnp.float32
    ).reshape(gathered.shape[0], -1)
    column_sums = lax.psum(column_terms, "head")
    attention = lax.all_to_all(
        column_sums.astype(jnp.bfloat16), "ez", split_axis=0, concat_axis=1, tiled=True
    )
    stream = resid.astype(jnp.float32) + attention.astype(jnp.float32)
    mean_square = jnp.mean(stream * stream, axis=1, keepdims=True)
    normed = (stream * lax.rsqrt(mean_square + norm_epsilon) * norm_gain).astype(jnp.bfloat16)
    expert_count = lax.axis_size("ez") * lax.axis_size("ey")
    top_count = route_ids.shape[1]
    capacity = max(2, -(-(seq_local * top_count) // expert_count))
    flat_ids = route_ids.reshape(-1)
    one_hot = (flat_ids[:, None] == jnp.arange(expert_count, dtype=jnp.int32)[None, :]).astype(
        jnp.int32
    )
    earlier = jnp.cumsum(one_hot, axis=0) - one_hot
    slot_index = jnp.sum(earlier * one_hot, axis=1)
    target = (flat_ids * capacity + slot_index).reshape(seq_local, top_count)
    places = jnp.arange(expert_count * capacity, dtype=jnp.int32)
    matches = target[None, :, :] == places[:, None, None]
    selector = jnp.sum(matches.astype(jnp.int32), axis=2).astype(jnp.bfloat16)
    blending = jnp.sum(jnp.where(matches, route_weights[None, :, :], 0.0), axis=2)
    gate_up = w_gate_up[0]
    col_width = stream.shape[1] // lax.axis_size("head")
    offset = lax.axis_index("head") * col_width
    normed_cols = lax.dynamic_slice_in_dim(normed, offset, col_width, 1)
    outgoing = jnp.dot(selector, normed_cols, preferred_element_type=jnp.float32).astype(jnp.bfloat16)
    outgoing = outgoing.reshape(expert_count, capacity, -1)
    arrived = lax.all_to_all(outgoing, EXPERT, split_axis=0, concat_axis=0, tiled=True)
    arrived_cols = arrived.reshape(-1, arrived.shape[2])
    flat_rows = lax.all_gather(arrived_cols, "head", axis=1, tiled=True)
    projected = jnp.einsum("rd,gfd->rgf", flat_rows, gate_up, preferred_element_type=jnp.float32)
    hidden = (jax.nn.silu(projected[:, 0]) * projected[:, 1]).astype(jnp.bfloat16)
    hidden_all = lax.all_gather(hidden, "head", axis=1, tiled=True)
    summed_cols = jnp.dot(hidden_all, down_cols, preferred_element_type=jnp.float32).astype(jnp.bfloat16)
    summed_rows = summed_cols.reshape(expert_count, capacity, -1)
    returned = lax.all_to_all(summed_rows, EXPERT, split_axis=0, concat_axis=0, tiled=True)
    back_rows = returned.reshape(expert_count * capacity, -1).astype(jnp.float32)
    mixture = jnp.dot(blending.T, back_rows, precision=lax.Precision.HIGHEST)
    stream_cols = lax.dynamic_slice_in_dim(stream, offset, col_width, 1)
    return stream_cols + mixture


def solution(mesh):
    placed = (
        P(EXPERT, "head", None),
        P(EXPERT, "head", None),
        P(EXPERT, None, None),
        P(EXPERT, None, None),
        P(EXPERT),
        P("head", EXPERT),
        P(EXPERT, None),
        P(),
        P(EXPERT, None),
        P(EXPERT, None),
        P(EXPERT, None, "head", None),
        P(EXPERT, "head", None),
    )
    head_count, expert_total = mesh.devices.shape
    y_count = len({device.coords[1] for device in mesh.devices[0]})
    split_mesh = Mesh(
        mesh.devices.reshape(head_count, expert_total // y_count, y_count), ("head",) + EXPERT
    )
    return jax.shard_map(
        on_device, mesh=split_mesh, in_specs=placed, out_specs=P(EXPERT, "head"), check_vma=False
    )
```

```python
import jax
import jax.numpy as jnp
from jax import lax
from jax.sharding import Mesh
from jax.sharding import PartitionSpec as P

EXPERT = ("ez", "ey")
softmax_scale = 192.0 ** (-0.5)
norm_epsilon = 1e-06


def attend(q_latent, q_rotary, cache_latent, cache_rotary, lengths):
    scores = jnp.einsum("shl,scl->shc", q_latent, cache_latent, preferred_element_type=jnp.float32)
    scores = scores + jnp.einsum(
        "shr,src->shc", q_rotary, cache_rotary, preferred_element_type=jnp.float32
    )
    scores = scores * softmax_scale
    position = lax.broadcasted_iota(jnp.int32, scores.shape, 2)
    scores = jnp.where(position < lengths[:, None, None], scores, -1e30)
    highest = jnp.max(scores, axis=2, keepdims=True)
    weights = jnp.exp(scores - highest)
    probs = (weights / jnp.sum(weights, axis=2, keepdims=True)).astype(jnp.bfloat16)
    return jnp.einsum(
        "shc,scl->shl", probs, cache_latent, preferred_element_type=jnp.float32
    ).astype(jnp.bfloat16)


def on_device(
    q_latent,
    q_rotary,
    cache_latent,
    cache_rotary,
    lengths,
    w_value_out,
    resid,
    norm_gain,
    route_ids,
    route_weights,
    w_gate_up,
    w_down,
):
    seq_local = q_latent.shape[0]
    latent_out = attend(q_latent, q_rotary, cache_latent, cache_rotary, lengths)
    flattened = latent_out.reshape(seq_local, -1)
    z_count = lax.axis_size("ez")
    latent_copies = jnp.broadcast_to(flattened[None], (z_count,) + flattened.shape)
    gathered = lax.all_to_all(latent_copies, "ez", split_axis=0, concat_axis=0, tiled=True)
    gathered = gathered.reshape(-1, flattened.shape[1])
    value_blocks = lax.all_gather(w_value_out, "ey", axis=0, tiled=False)
    column_terms = jnp.einsum(
        "sk,jkc->sjc", gathered, value_blocks, preferred_element_type=jnp.float32
    ).reshape(gathered.shape[0], -1)
    column_sums = lax.psum(column_terms, "head")
    attention = lax.all_to_all(
        column_sums.astype(jnp.bfloat16), "ez", split_axis=0, concat_axis=1, tiled=True
    )
    stream = resid.astype(jnp.float32) + attention.astype(jnp.float32)
    mean_square = jnp.mean(stream * stream, axis=1, keepdims=True)
    normed = (stream * lax.rsqrt(mean_square + norm_epsilon) * norm_gain).astype(jnp.bfloat16)
    expert_count = lax.axis_size("ez") * lax.axis_size("ey")
    top_count = route_ids.shape[1]
    capacity = max(2, -(-(seq_local * top_count) // expert_count))
    flat_ids = route_ids.reshape(-1)
    one_hot = (flat_ids[:, None] == jnp.arange(expert_count, dtype=jnp.int32)[None, :]).astype(
        jnp.int32
    )
    earlier = jnp.cumsum(one_hot, axis=0) - one_hot
    slot_index = jnp.sum(earlier * one_hot, axis=1)
    target = (flat_ids * capacity + slot_index).reshape(seq_local, top_count)
    places = jnp.arange(expert_count * capacity, dtype=jnp.int32)
    matches = target[None, :, :] == places[:, None, None]
    selector = jnp.sum(matches.astype(jnp.int32), axis=2).astype(jnp.bfloat16)
    blending = jnp.sum(jnp.where(matches, route_weights[None, :, :], 0.0), axis=2)
    gate_up = w_gate_up[0]
    col_width = stream.shape[1] // lax.axis_size("head")
    offset = lax.axis_index("head") * col_width
    normed_cols = lax.dynamic_slice_in_dim(normed, offset, col_width, 1)
    outgoing = jnp.dot(selector, normed_cols, preferred_element_type=jnp.float32).astype(jnp.bfloat16)
    outgoing = outgoing.reshape(expert_count, capacity, -1)
    arrived = lax.all_to_all(outgoing, EXPERT, split_axis=0, concat_axis=0, tiled=True)
    arrived_cols = arrived.reshape(-1, arrived.shape[2])
    head_count = lax.axis_size("head")
    down_blocks = w_down[0].reshape(w_down.shape[1], head_count, -1)
    arrived_cols, down_blocks = lax.optimization_barrier((arrived_cols, down_blocks))
    down_cols = lax.all_to_all(down_blocks, "head", split_axis=1, concat_axis=0, tiled=True)
    down_cols = down_cols.reshape(-1, down_blocks.shape[2])
    flat_rows = lax.all_gather(arrived_cols, "head", axis=1, tiled=True)
    projected = jnp.einsum("rd,gfd->rgf", flat_rows, gate_up, preferred_element_type=jnp.float32)
    hidden = (jax.nn.silu(projected[:, 0]) * projected[:, 1]).astype(jnp.bfloat16)
    hidden_all = lax.all_gather(hidden, "head", axis=1, tiled=True)
    summed_cols = jnp.dot(hidden_all, down_cols, preferred_element_type=jnp.float32).astype(jnp.bfloat16)
    summed_rows = summed_cols.reshape(expert_count, capacity, -1)
    returned = lax.all_to_all(summed_rows, EXPERT, split_axis=0, concat_axis=0, tiled=True)
    back_rows = returned.reshape(expert_count * capacity, -1).astype(jnp.float32)
    mixture = jnp.dot(blending.T, back_rows, precision=lax.Precision.HIGHEST)
    stream_cols = lax.dynamic_slice_in_dim(stream, offset, col_width, 1)
    return stream_cols + mixture


def solution(mesh):
    placed = (
        P(EXPERT, "head", None),
        P(EXPERT, "head", None),
        P(EXPERT, None, None),
        P(EXPERT, None, None),
        P(EXPERT),
        P("head", EXPERT),
        P(EXPERT, None),
        P(),
        P(EXPERT, None),
        P(EXPERT, None),
        P(EXPERT, None, "head", None),
        P(EXPERT, "head", None),
    )
    head_count, expert_total = mesh.devices.shape
    y_count = len({device.coords[1] for device in mesh.devices[0]})
    split_mesh = Mesh(
        mesh.devices.reshape(head_count, expert_total // y_count, y_count), ("head",) + EXPERT
    )
    return jax.shard_map(
        on_device, mesh=split_mesh, in_specs=placed, out_specs=P(EXPERT, "head"), check_vma=False
    )
```

```python
import jax
import jax.numpy as jnp
from jax import lax
from jax.sharding import Mesh
from jax.sharding import PartitionSpec as P

EXPERT = ("ez", "ey")
softmax_scale = 192.0 ** (-0.5)
norm_epsilon = 1e-06


def attend(q_latent, q_rotary, cache_latent, cache_rotary, lengths):
    scores = jnp.einsum("shl,scl->shc", q_latent, cache_latent, preferred_element_type=jnp.float32)
    scores = scores + jnp.einsum(
        "shr,src->shc", q_rotary, cache_rotary, preferred_element_type=jnp.float32
    )
    scores = scores * softmax_scale
    position = lax.broadcasted_iota(jnp.int32, scores.shape, 2)
    scores = jnp.where(position < lengths[:, None, None], scores, -1e30)
    highest = jnp.max(scores, axis=2, keepdims=True)
    weights = jnp.exp(scores - highest)
    probs = (weights / jnp.sum(weights, axis=2, keepdims=True)).astype(jnp.bfloat16)
    return jnp.einsum(
        "shc,scl->shl", probs, cache_latent, preferred_element_type=jnp.float32
    ).astype(jnp.bfloat16)


def on_device(
    q_latent,
    q_rotary,
    cache_latent,
    cache_rotary,
    lengths,
    w_value_out,
    resid,
    norm_gain,
    route_ids,
    route_weights,
    w_gate_up,
    w_down,
):
    seq_local = q_latent.shape[0]
    latent_out = attend(q_latent, q_rotary, cache_latent, cache_rotary, lengths)
    flattened = latent_out.reshape(seq_local, -1)
    z_count = lax.axis_size("ez")
    latent_copies = jnp.broadcast_to(flattened[None], (z_count,) + flattened.shape)
    gathered = lax.all_to_all(latent_copies, "ez", split_axis=0, concat_axis=0, tiled=True)
    gathered = gathered.reshape(-1, flattened.shape[1])
    value_cols = lax.all_gather(w_value_out, "ey", axis=1, tiled=True)
    column_terms = jnp.dot(gathered, value_cols, preferred_element_type=jnp.float32)
    column_sums = lax.psum(column_terms, "head")
    attention = lax.all_to_all(
        column_sums.astype(jnp.bfloat16), "ez", split_axis=0, concat_axis=1, tiled=True
    )
    stream = resid.astype(jnp.float32) + attention.astype(jnp.float32)
    mean_square = jnp.mean(stream * stream, axis=1, keepdims=True)
    normed = (stream * lax.rsqrt(mean_square + norm_epsilon) * norm_gain).astype(jnp.bfloat16)
    expert_count = lax.axis_size("ez") * lax.axis_size("ey")
    top_count = route_ids.shape[1]
    capacity = max(2, -(-(seq_local * top_count) // expert_count))
    flat_ids = route_ids.reshape(-1)
    one_hot = (flat_ids[:, None] == jnp.arange(expert_count, dtype=jnp.int32)[None, :]).astype(
        jnp.int32
    )
    earlier = jnp.cumsum(one_hot, axis=0) - one_hot
    slot_index = jnp.sum(earlier * one_hot, axis=1)
    target = (flat_ids * capacity + slot_index).reshape(seq_local, top_count)
    places = jnp.arange(expert_count * capacity, dtype=jnp.int32)
    matches = target[None, :, :] == places[:, None, None]
    selector = jnp.sum(matches.astype(jnp.int32), axis=2).astype(jnp.bfloat16)
    blending = jnp.sum(jnp.where(matches, route_weights[None, :, :], 0.0), axis=2)
    gate_up = w_gate_up[0]
    col_width = stream.shape[1] // lax.axis_size("head")
    offset = lax.axis_index("head") * col_width
    normed_cols = lax.dynamic_slice_in_dim(normed, offset, col_width, 1)
    outgoing = jnp.dot(selector, normed_cols, preferred_element_type=jnp.float32).astype(jnp.bfloat16)
    outgoing = outgoing.reshape(expert_count, capacity, -1)
    arrived = lax.all_to_all(outgoing, EXPERT, split_axis=0, concat_axis=0, tiled=True)
    arrived_cols = arrived.reshape(-1, arrived.shape[2])
    head_count = lax.axis_size("head")
    down_blocks = w_down[0].reshape(w_down.shape[1], head_count, -1)
    arrived_cols, down_blocks = lax.optimization_barrier((arrived_cols, down_blocks))
    down_cols = lax.all_to_all(down_blocks, "head", split_axis=1, concat_axis=0, tiled=True)
    down_cols = down_cols.reshape(-1, down_blocks.shape[2])
    flat_rows = lax.all_gather(arrived_cols, "head", axis=1, tiled=True)
    projected = jnp.einsum("rd,gfd->rgf", flat_rows, gate_up, preferred_element_type=jnp.float32)
    hidden = (jax.nn.silu(projected[:, 0]) * projected[:, 1]).astype(jnp.bfloat16)
    hidden_all = lax.all_gather(hidden, "head", axis=1, tiled=True)
    summed_cols = jnp.dot(hidden_all, down_cols, preferred_element_type=jnp.float32).astype(jnp.bfloat16)
    summed_rows = summed_cols.reshape(expert_count, capacity, -1)
    returned = lax.all_to_all(summed_rows, EXPERT, split_axis=0, concat_axis=0, tiled=True)
    back_rows = returned.reshape(expert_count * capacity, -1).astype(jnp.float32)
    mixture = jnp.dot(blending.T, back_rows, precision=lax.Precision.HIGHEST)
    stream_cols = lax.dynamic_slice_in_dim(stream, offset, col_width, 1)
    return stream_cols + mixture


def solution(mesh):
    placed = (
        P(EXPERT, "head", None),
        P(EXPERT, "head", None),
        P(EXPERT, None, None),
        P(EXPERT, None, None),
        P(EXPERT),
        P("head", EXPERT),
        P(EXPERT, None),
        P(),
        P(EXPERT, None),
        P(EXPERT, None),
        P(EXPERT, None, "head", None),
        P(EXPERT, "head", None),
    )
    head_count, expert_total = mesh.devices.shape
    y_count = len({device.coords[1] for device in mesh.devices[0]})
    split_mesh = Mesh(
        mesh.devices.reshape(head_count, expert_total // y_count, y_count), ("head",) + EXPERT
    )
    return jax.shard_map(
        on_device, mesh=split_mesh, in_specs=placed, out_specs=P(EXPERT, "head"), check_vma=False
    )
```

```python
import jax
import jax.numpy as jnp
from jax import lax
from jax.sharding import Mesh
from jax.sharding import PartitionSpec as P

EXPERT = ("ez", "ey")
softmax_scale = 192.0 ** (-0.5)
norm_epsilon = 1e-06


def attend(q_latent, q_rotary, cache_latent, cache_rotary, lengths):
    scores = jnp.einsum("shl,scl->shc", q_latent, cache_latent, preferred_element_type=jnp.float32)
    scores = scores + jnp.einsum(
        "shr,src->shc", q_rotary, cache_rotary, preferred_element_type=jnp.float32
    )
    scores = scores * softmax_scale
    position = lax.broadcasted_iota(jnp.int32, scores.shape, 2)
    scores = jnp.where(position < lengths[:, None, None], scores, -1e30)
    highest = jnp.max(scores, axis=2, keepdims=True)
    weights = jnp.exp(scores - highest)
    probs = (weights / jnp.sum(weights, axis=2, keepdims=True)).astype(jnp.bfloat16)
    return jnp.einsum(
        "shc,scl->shl", probs, cache_latent, preferred_element_type=jnp.float32
    ).astype(jnp.bfloat16)


def on_device(
    q_latent,
    q_rotary,
    cache_latent,
    cache_rotary,
    lengths,
    w_value_out,
    resid,
    norm_gain,
    route_ids,
    route_weights,
    w_gate_up,
    w_down,
):
    seq_local = q_latent.shape[0]
    latent_out = attend(q_latent, q_rotary, cache_latent, cache_rotary, lengths)
    flattened = latent_out.reshape(seq_local, -1)
    z_count = lax.axis_size("ez")
    forward = [(i, (i + 1) % z_count) for i in range(z_count)]
    backward = [(i, (i - 1) % z_count) for i in range(z_count)]
    ahead, behind = [], []
    moving_fwd, moving_bwd = flattened, flattened
    for step in range(1, z_count // 2 + 1):
        moving_fwd = lax.ppermute(moving_fwd, "ez", forward)
        behind.append(moving_fwd)
        if step < z_count - step:
            moving_bwd = lax.ppermute(moving_bwd, "ez", backward)
            ahead.append(moving_bwd)
    relative = [flattened] + ahead + behind[len(ahead):] + behind[: len(ahead)][::-1]
    gathered = jnp.concatenate(relative, axis=0)
    value_cols = lax.all_gather(w_value_out, "ey", axis=1, tiled=True)
    column_terms = jnp.dot(gathered, value_cols, preferred_element_type=jnp.float32)
    column_terms = column_terms.reshape(z_count, seq_local, -1)
    column_terms = jnp.roll(column_terms, lax.axis_index("ez"), axis=0)
    column_terms = column_terms.reshape(z_count * seq_local, -1)
    column_sums = lax.psum(column_terms, "head")
    attention = lax.all_to_all(
        column_sums.astype(jnp.bfloat16), "ez", split_axis=0, concat_axis=1, tiled=True
    )
    stream = resid.astype(jnp.float32) + attention.astype(jnp.float32)
    mean_square = jnp.mean(stream * stream, axis=1, keepdims=True)
    normed = (stream * lax.rsqrt(mean_square + norm_epsilon) * norm_gain).astype(jnp.bfloat16)
    expert_count = lax.axis_size("ez") * lax.axis_size("ey")
    top_count = route_ids.shape[1]
    capacity = max(2, -(-(seq_local * top_count) // expert_count))
    flat_ids = route_ids.reshape(-1)
    one_hot = (flat_ids[:, None] == jnp.arange(expert_count, dtype=jnp.int32)[None, :]).astype(
        jnp.int32
    )
    earlier = jnp.cumsum(one_hot, axis=0) - one_hot
    slot_index = jnp.sum(earlier * one_hot, axis=1)
    target = (flat_ids * capacity + slot_index).reshape(seq_local, top_count)
    places = jnp.arange(expert_count * capacity, dtype=jnp.int32)
    matches = target[None, :, :] == places[:, None, None]
    selector = jnp.sum(matches.astype(jnp.int32), axis=2).astype(jnp.bfloat16)
    blending = jnp.sum(jnp.where(matches, route_weights[None, :, :], 0.0), axis=2)
    gate_up = w_gate_up[0]
    col_width = stream.shape[1] // lax.axis_size("head")
    offset = lax.axis_index("head") * col_width
    normed_cols = lax.dynamic_slice_in_dim(normed, offset, col_width, 1)
    outgoing = jnp.dot(selector, normed_cols, preferred_element_type=jnp.float32).astype(jnp.bfloat16)
    outgoing = outgoing.reshape(expert_count, capacity, -1)
    arrived = lax.all_to_all(outgoing, EXPERT, split_axis=0, concat_axis=0, tiled=True)
    arrived_cols = arrived.reshape(-1, arrived.shape[2])
    head_count = lax.axis_size("head")
    down_blocks = w_down[0].reshape(w_down.shape[1], head_count, -1)
    arrived_cols, down_blocks = lax.optimization_barrier((arrived_cols, down_blocks))
    down_cols = lax.all_to_all(down_blocks, "head", split_axis=1, concat_axis=0, tiled=True)
    down_cols = down_cols.reshape(-1, down_blocks.shape[2])
    flat_rows = lax.all_gather(arrived_cols, "head", axis=1, tiled=True)
    projected = jnp.einsum("rd,gfd->rgf", flat_rows, gate_up, preferred_element_type=jnp.float32)
    hidden = (jax.nn.silu(projected[:, 0]) * projected[:, 1]).astype(jnp.bfloat16)
    hidden_all = lax.all_gather(hidden, "head", axis=1, tiled=True)
    summed_cols = jnp.dot(hidden_all, down_cols, preferred_element_type=jnp.float32).astype(jnp.bfloat16)
    summed_rows = summed_cols.reshape(expert_count, capacity, -1)
    returned = lax.all_to_all(summed_rows, EXPERT, split_axis=0, concat_axis=0, tiled=True)
    back_rows = returned.reshape(expert_count * capacity, -1).astype(jnp.float32)
    mixture = jnp.dot(blending.T, back_rows, precision=lax.Precision.HIGHEST)
    stream_cols = lax.dynamic_slice_in_dim(stream, offset, col_width, 1)
    return stream_cols + mixture


def solution(mesh):
    placed = (
        P(EXPERT, "head", None),
        P(EXPERT, "head", None),
        P(EXPERT, None, None),
        P(EXPERT, None, None),
        P(EXPERT),
        P("head", EXPERT),
        P(EXPERT, None),
        P(),
        P(EXPERT, None),
        P(EXPERT, None),
        P(EXPERT, None, "head", None),
        P(EXPERT, "head", None),
    )
    head_count, expert_total = mesh.devices.shape
    y_count = len({device.coords[1] for device in mesh.devices[0]})
    split_mesh = Mesh(
        mesh.devices.reshape(head_count, expert_total // y_count, y_count), ("head",) + EXPERT
    )
    return jax.shard_map(
        on_device, mesh=split_mesh, in_specs=placed, out_specs=P(EXPERT, "head"), check_vma=False
    )
```

```python
import jax
import jax.numpy as jnp
from jax import lax
from jax.sharding import Mesh
from jax.sharding import PartitionSpec as P

EXPERT = ("ez", "ey")
softmax_scale = 192.0 ** (-0.5)
norm_epsilon = 1e-06


def attend(q_latent, q_rotary, cache_latent, cache_rotary, lengths):
    scores = jnp.einsum("shl,scl->shc", q_latent, cache_latent, preferred_element_type=jnp.float32)
    scores = scores + jnp.einsum(
        "shr,src->shc", q_rotary, cache_rotary, preferred_element_type=jnp.float32
    )
    scores = scores * softmax_scale
    position = lax.broadcasted_iota(jnp.int32, scores.shape, 2)
    scores = jnp.where(position < lengths[:, None, None], scores, -1e30)
    highest = jnp.max(scores, axis=2, keepdims=True)
    weights = jnp.exp(scores - highest)
    probs = (weights / jnp.sum(weights, axis=2, keepdims=True)).astype(jnp.bfloat16)
    return jnp.einsum(
        "shc,scl->shl", probs, cache_latent, preferred_element_type=jnp.float32
    ).astype(jnp.bfloat16)


def on_device(
    q_latent,
    q_rotary,
    cache_latent,
    cache_rotary,
    lengths,
    w_value_out,
    resid,
    norm_gain,
    route_ids,
    route_weights,
    w_gate_up,
    w_down,
):
    seq_local = q_latent.shape[0]
    latent_out = attend(q_latent, q_rotary, cache_latent, cache_rotary, lengths)
    flattened = latent_out.reshape(seq_local, -1)
    z_count = lax.axis_size("ez")
    forward = [(i, (i + 1) % z_count) for i in range(z_count)]
    backward = [(i, (i - 1) % z_count) for i in range(z_count)]
    ahead, behind = [], []
    moving_fwd, moving_bwd = flattened, flattened
    for step in range(1, z_count // 2 + 1):
        moving_fwd = lax.ppermute(moving_fwd, "ez", forward)
        behind.append(moving_fwd)
        if step < z_count - step:
            moving_bwd = lax.ppermute(moving_bwd, "ez", backward)
            ahead.append(moving_bwd)
    relative = [flattened] + ahead + behind[len(ahead):] + behind[: len(ahead)][::-1]
    relative = list(lax.optimization_barrier(tuple(relative)))
    gathered = jnp.concatenate(relative, axis=0)
    value_cols = lax.all_gather(w_value_out, "ey", axis=1, tiled=True)
    column_terms = jnp.dot(gathered, value_cols, preferred_element_type=jnp.float32)
    column_terms = column_terms.reshape(z_count, seq_local, -1)
    column_terms = jnp.roll(column_terms, lax.axis_index("ez"), axis=0)
    column_terms = column_terms.reshape(z_count * seq_local, -1)
    column_sums = lax.psum(column_terms, "head")
    attention = lax.all_to_all(
        column_sums.astype(jnp.bfloat16), "ez", split_axis=0, concat_axis=1, tiled=True
    )
    stream = resid.astype(jnp.float32) + attention.astype(jnp.float32)
    mean_square = jnp.mean(stream * stream, axis=1, keepdims=True)
    normed = (stream * lax.rsqrt(mean_square + norm_epsilon) * norm_gain).astype(jnp.bfloat16)
    expert_count = lax.axis_size("ez") * lax.axis_size("ey")
    top_count = route_ids.shape[1]
    capacity = max(2, -(-(seq_local * top_count) // expert_count))
    flat_ids = route_ids.reshape(-1)
    one_hot = (flat_ids[:, None] == jnp.arange(expert_count, dtype=jnp.int32)[None, :]).astype(
        jnp.int32
    )
    earlier = jnp.cumsum(one_hot, axis=0) - one_hot
    slot_index = jnp.sum(earlier * one_hot, axis=1)
    target = (flat_ids * capacity + slot_index).reshape(seq_local, top_count)
    places = jnp.arange(expert_count * capacity, dtype=jnp.int32)
    matches = target[None, :, :] == places[:, None, None]
    selector = jnp.sum(matches.astype(jnp.int32), axis=2).astype(jnp.bfloat16)
    blending = jnp.sum(jnp.where(matches, route_weights[None, :, :], 0.0), axis=2)
    gate_up = w_gate_up[0]
    col_width = stream.shape[1] // lax.axis_size("head")
    offset = lax.axis_index("head") * col_width
    normed_cols = lax.dynamic_slice_in_dim(normed, offset, col_width, 1)
    outgoing = jnp.dot(selector, normed_cols, preferred_element_type=jnp.float32).astype(jnp.bfloat16)
    outgoing = outgoing.reshape(expert_count, capacity, -1)
    arrived = lax.all_to_all(outgoing, EXPERT, split_axis=0, concat_axis=0, tiled=True)
    arrived_cols = arrived.reshape(-1, arrived.shape[2])
    head_count = lax.axis_size("head")
    down_blocks = w_down[0].reshape(w_down.shape[1], head_count, -1)
    arrived_cols, down_blocks = lax.optimization_barrier((arrived_cols, down_blocks))
    down_cols = lax.all_to_all(down_blocks, "head", split_axis=1, concat_axis=0, tiled=True)
    down_cols = down_cols.reshape(-1, down_blocks.shape[2])
    flat_rows = lax.all_gather(arrived_cols, "head", axis=1, tiled=True)
    projected = jnp.einsum("rd,gfd->rgf", flat_rows, gate_up, preferred_element_type=jnp.float32)
    hidden = (jax.nn.silu(projected[:, 0]) * projected[:, 1]).astype(jnp.bfloat16)
    hidden_all = lax.all_gather(hidden, "head", axis=1, tiled=True)
    summed_cols = jnp.dot(hidden_all, down_cols, preferred_element_type=jnp.float32).astype(jnp.bfloat16)
    summed_rows = summed_cols.reshape(expert_count, capacity, -1)
    returned = lax.all_to_all(summed_rows, EXPERT, split_axis=0, concat_axis=0, tiled=True)
    back_rows = returned.reshape(expert_count * capacity, -1).astype(jnp.float32)
    mixture = jnp.dot(blending.T, back_rows, precision=lax.Precision.HIGHEST)
    stream_cols = lax.dynamic_slice_in_dim(stream, offset, col_width, 1)
    return stream_cols + mixture


def solution(mesh):
    placed = (
        P(EXPERT, "head", None),
        P(EXPERT, "head", None),
        P(EXPERT, None, None),
        P(EXPERT, None, None),
        P(EXPERT),
        P("head", EXPERT),
        P(EXPERT, None),
        P(),
        P(EXPERT, None),
        P(EXPERT, None),
        P(EXPERT, None, "head", None),
        P(EXPERT, "head", None),
    )
    head_count, expert_total = mesh.devices.shape
    y_count = len({device.coords[1] for device in mesh.devices[0]})
    split_mesh = Mesh(
        mesh.devices.reshape(head_count, expert_total // y_count, y_count), ("head",) + EXPERT
    )
    return jax.shard_map(
        on_device, mesh=split_mesh, in_specs=placed, out_specs=P(EXPERT, "head"), check_vma=False
    )
```

```python
import jax
import jax.numpy as jnp
from jax import lax
from jax.sharding import Mesh
from jax.sharding import PartitionSpec as P

EXPERT = ("ez", "ey")
softmax_scale = 192.0 ** (-0.5)
norm_epsilon = 1e-06


def attend(q_latent, q_rotary, cache_latent, cache_rotary, lengths):
    scores = jnp.einsum("shl,scl->shc", q_latent, cache_latent, preferred_element_type=jnp.float32)
    scores = scores + jnp.einsum(
        "shr,src->shc", q_rotary, cache_rotary, preferred_element_type=jnp.float32
    )
    scores = scores * softmax_scale
    position = lax.broadcasted_iota(jnp.int32, scores.shape, 2)
    scores = jnp.where(position < lengths[:, None, None], scores, -1e30)
    highest = jnp.max(scores, axis=2, keepdims=True)
    weights = jnp.exp(scores - highest)
    probs = (weights / jnp.sum(weights, axis=2, keepdims=True)).astype(jnp.bfloat16)
    return jnp.einsum(
        "shc,scl->shl", probs, cache_latent, preferred_element_type=jnp.float32
    ).astype(jnp.bfloat16)


def on_device(
    q_latent,
    q_rotary,
    cache_latent,
    cache_rotary,
    lengths,
    w_value_out,
    resid,
    norm_gain,
    route_ids,
    route_weights,
    w_gate_up,
    w_down,
):
    seq_local = q_latent.shape[0]
    latent_out = attend(q_latent, q_rotary, cache_latent, cache_rotary, lengths)
    flattened = latent_out.reshape(seq_local, -1)
    z_count = lax.axis_size("ez")
    latent_copies = jnp.broadcast_to(flattened[None], (z_count,) + flattened.shape)
    gathered = lax.all_to_all(latent_copies, "ez", split_axis=0, concat_axis=0, tiled=True)
    gathered = gathered.reshape(-1, flattened.shape[1])
    value_cols = lax.all_gather(w_value_out, "ey", axis=1, tiled=True)
    column_terms = jnp.dot(gathered, value_cols, preferred_element_type=jnp.float32)
    head_count = lax.axis_size("head")
    head_index = lax.axis_index("head")
    z_count = lax.axis_size("ez")
    width = resid.shape[1]
    block = column_terms.shape[1]
    piece = block // head_count
    sending = column_terms.reshape(z_count, seq_local, head_count, piece)
    sending = sending.transpose(2, 0, 1, 3).reshape(head_count * z_count, seq_local, piece)
    received = lax.all_to_all(sending, ("head", "ez"), split_axis=0, concat_axis=0, tiled=True)
    received = received.reshape(head_count, z_count, seq_local, piece)
    attention = jnp.sum(received, axis=0).astype(jnp.bfloat16)
    attention = attention.transpose(1, 0, 2).reshape(seq_local, -1)
    strided = lambda values: lax.dynamic_index_in_dim(
        values.reshape(values.shape[:-1] + (width // block, head_count, piece)),
        head_index, axis=values.ndim, keepdims=False,
    ).reshape(values.shape[:-1] + (-1,))
    stream_part = strided(resid).astype(jnp.float32) + attention.astype(jnp.float32)
    square_sum = lax.psum(jnp.sum(stream_part * stream_part, axis=1, keepdims=True), "head")
    mean_square = square_sum / width
    normed_part = (stream_part * lax.rsqrt(mean_square + norm_epsilon) * strided(norm_gain)).astype(
        jnp.bfloat16
    )
    halves = width // (head_count * block)
    to_heads = stream_part.reshape(seq_local, head_count, halves, piece).transpose(1, 0, 2, 3)
    from_heads = lax.all_to_all(to_heads, "head", split_axis=0, concat_axis=0, tiled=True)
    stream_cols = from_heads.transpose(1, 2, 0, 3).reshape(seq_local, -1)
    expert_count = lax.axis_size("ez") * lax.axis_size("ey")
    top_count = route_ids.shape[1]
    capacity = max(2, -(-(seq_local * top_count) // expert_count))
    flat_ids = route_ids.reshape(-1)
    one_hot = (flat_ids[:, None] == jnp.arange(expert_count, dtype=jnp.int32)[None, :]).astype(
        jnp.int32
    )
    earlier = jnp.cumsum(one_hot, axis=0) - one_hot
    slot_index = jnp.sum(earlier * one_hot, axis=1)
    target = (flat_ids * capacity + slot_index).reshape(seq_local, top_count)
    places = jnp.arange(expert_count * capacity, dtype=jnp.int32)
    matches = target[None, :, :] == places[:, None, None]
    selector = jnp.sum(matches.astype(jnp.int32), axis=2).astype(jnp.bfloat16)
    blending = jnp.sum(jnp.where(matches, route_weights[None, :, :], 0.0), axis=2)
    gate_up = w_gate_up[0].reshape(
        w_gate_up.shape[1], w_gate_up.shape[2], width // block, head_count, piece
    )
    gate_up = gate_up.transpose(0, 1, 3, 2, 4).reshape(w_gate_up.shape[1], w_gate_up.shape[2], width)
    outgoing = jnp.dot(selector, normed_part, preferred_element_type=jnp.float32).astype(jnp.bfloat16)
    outgoing = outgoing.reshape(expert_count, capacity, -1)
    arrived = lax.all_to_all(outgoing, EXPERT, split_axis=0, concat_axis=0, tiled=True)
    arrived_cols = arrived.reshape(-1, arrived.shape[2])
    head_count = lax.axis_size("head")
    down_blocks = w_down[0].reshape(w_down.shape[1], head_count, -1)
    arrived_cols, down_blocks = lax.optimization_barrier((arrived_cols, down_blocks))
    down_cols = lax.all_to_all(down_blocks, "head", split_axis=1, concat_axis=0, tiled=True)
    down_cols = down_cols.reshape(-1, down_blocks.shape[2])
    flat_rows = lax.all_gather(arrived_cols, "head", axis=1, tiled=True)
    projected = jnp.einsum("rd,gfd->rgf", flat_rows, gate_up, preferred_element_type=jnp.float32)
    hidden = (jax.nn.silu(projected[:, 0]) * projected[:, 1]).astype(jnp.bfloat16)
    hidden_all = lax.all_gather(hidden, "head", axis=1, tiled=True)
    summed_cols = jnp.dot(hidden_all, down_cols, preferred_element_type=jnp.float32).astype(jnp.bfloat16)
    summed_rows = summed_cols.reshape(expert_count, capacity, -1)
    returned = lax.all_to_all(summed_rows, EXPERT, split_axis=0, concat_axis=0, tiled=True)
    back_rows = returned.reshape(expert_count * capacity, -1).astype(jnp.float32)
    mixture = jnp.dot(blending.T, back_rows, precision=lax.Precision.HIGHEST)
    return stream_cols + mixture


def solution(mesh):
    placed = (
        P(EXPERT, "head", None),
        P(EXPERT, "head", None),
        P(EXPERT, None, None),
        P(EXPERT, None, None),
        P(EXPERT),
        P("head", EXPERT),
        P(EXPERT, None),
        P(),
        P(EXPERT, None),
        P(EXPERT, None),
        P(EXPERT, None, "head", None),
        P(EXPERT, "head", None),
    )
    head_count, expert_total = mesh.devices.shape
    y_count = len({device.coords[1] for device in mesh.devices[0]})
    split_mesh = Mesh(
        mesh.devices.reshape(head_count, expert_total // y_count, y_count), ("head",) + EXPERT
    )
    return jax.shard_map(
        on_device, mesh=split_mesh, in_specs=placed, out_specs=P(EXPERT, "head"), check_vma=False
    )
```

```python
import jax
import jax.numpy as jnp
from jax import lax
from jax.sharding import Mesh
from jax.sharding import PartitionSpec as P

EXPERT = ("ez", "ey")
softmax_scale = 192.0 ** (-0.5)
norm_epsilon = 1e-06


def attend(q_latent, q_rotary, cache_latent, cache_rotary, lengths):
    scores = jnp.einsum("shl,scl->shc", q_latent, cache_latent, preferred_element_type=jnp.float32)
    scores = scores + jnp.einsum(
        "shr,src->shc", q_rotary, cache_rotary, preferred_element_type=jnp.float32
    )
    scores = scores * softmax_scale
    position = lax.broadcasted_iota(jnp.int32, scores.shape, 2)
    scores = jnp.where(position < lengths[:, None, None], scores, -1e30)
    highest = jnp.max(scores, axis=2, keepdims=True)
    weights = jnp.exp(scores - highest)
    probs = (weights / jnp.sum(weights, axis=2, keepdims=True)).astype(jnp.bfloat16)
    return jnp.einsum(
        "shc,scl->shl", probs, cache_latent, preferred_element_type=jnp.float32
    ).astype(jnp.bfloat16)


def on_device(
    q_latent,
    q_rotary,
    cache_latent,
    cache_rotary,
    lengths,
    w_value_out,
    resid,
    norm_gain,
    route_ids,
    route_weights,
    w_gate_up,
    w_down,
):
    seq_local = q_latent.shape[0]
    latent_out = attend(q_latent, q_rotary, cache_latent, cache_rotary, lengths)
    flattened = latent_out.reshape(seq_local, -1)
    z_count = lax.axis_size("ez")
    latent_copies = jnp.broadcast_to(flattened[None], (z_count,) + flattened.shape)
    gathered = lax.all_to_all(latent_copies, "ez", split_axis=0, concat_axis=0, tiled=True)
    gathered = gathered.reshape(-1, flattened.shape[1])
    value_cols = lax.all_gather(w_value_out, "ey", axis=1, tiled=True)
    width = resid.shape[1]
    block = value_cols.shape[1]
    head_count = lax.axis_size("head")
    piece = block // head_count
    gate_up = w_gate_up[0].reshape(
        w_gate_up.shape[1], w_gate_up.shape[2], width // block, head_count, piece
    )
    gate_up = gate_up.transpose(0, 1, 3, 2, 4).reshape(w_gate_up.shape[1], w_gate_up.shape[2], width)
    gathered, gate_up = lax.optimization_barrier((gathered, gate_up))
    column_terms = jnp.dot(gathered, value_cols, preferred_element_type=jnp.float32)
    head_count = lax.axis_size("head")
    head_index = lax.axis_index("head")
    z_count = lax.axis_size("ez")
    width = resid.shape[1]
    block = column_terms.shape[1]
    piece = block // head_count
    sending = column_terms.reshape(z_count, seq_local, head_count, piece)
    sending = sending.transpose(2, 0, 1, 3).reshape(head_count * z_count, seq_local, piece)
    received = lax.all_to_all(sending, ("head", "ez"), split_axis=0, concat_axis=0, tiled=True)
    received = received.reshape(head_count, z_count, seq_local, piece)
    attention = jnp.sum(received, axis=0).astype(jnp.bfloat16)
    attention = attention.transpose(1, 0, 2).reshape(seq_local, -1)
    strided = lambda values: lax.dynamic_index_in_dim(
        values.reshape(values.shape[:-1] + (width // block, head_count, piece)),
        head_index, axis=values.ndim, keepdims=False,
    ).reshape(values.shape[:-1] + (-1,))
    stream_part = strided(resid).astype(jnp.float32) + attention.astype(jnp.float32)
    square_sum = lax.psum(jnp.sum(stream_part * stream_part, axis=1, keepdims=True), "head")
    mean_square = square_sum / width
    normed_part = (stream_part * lax.rsqrt(mean_square + norm_epsilon) * strided(norm_gain)).astype(
        jnp.bfloat16
    )
    expert_count = lax.axis_size("ez") * lax.axis_size("ey")
    top_count = route_ids.shape[1]
    capacity = max(2, -(-(seq_local * top_count) // expert_count))
    flat_ids = route_ids.reshape(-1)
    one_hot = (flat_ids[:, None] == jnp.arange(expert_count, dtype=jnp.int32)[None, :]).astype(
        jnp.int32
    )
    earlier = jnp.cumsum(one_hot, axis=0) - one_hot
    slot_index = jnp.sum(earlier * one_hot, axis=1)
    target = (flat_ids * capacity + slot_index).reshape(seq_local, top_count)
    places = jnp.arange(expert_count * capacity, dtype=jnp.int32)
    matches = target[None, :, :] == places[:, None, None]
    selector = jnp.sum(matches.astype(jnp.int32), axis=2).astype(jnp.bfloat16)
    blending = jnp.sum(jnp.where(matches, route_weights[None, :, :], 0.0), axis=2)
    outgoing = jnp.dot(selector, normed_part, preferred_element_type=jnp.float32).astype(jnp.bfloat16)
    outgoing = outgoing.reshape(expert_count, capacity, -1)
    arrived = lax.all_to_all(outgoing, EXPERT, split_axis=0, concat_axis=0, tiled=True)
    arrived_cols = arrived.reshape(-1, arrived.shape[2])
    head_count = lax.axis_size("head")
    down_blocks = w_down[0].reshape(w_down.shape[1], head_count, -1)
    halves = width // (head_count * block)
    to_heads = stream_part.reshape(seq_local, head_count, halves, piece).transpose(1, 0, 2, 3)
    arrived_cols, down_blocks, to_heads = lax.optimization_barrier((arrived_cols, down_blocks, to_heads))
    from_heads = lax.all_to_all(to_heads, "head", split_axis=0, concat_axis=0, tiled=True)
    stream_cols = from_heads.transpose(1, 2, 0, 3).reshape(seq_local, -1)
    down_cols = lax.all_to_all(down_blocks, "head", split_axis=1, concat_axis=0, tiled=True)
    down_cols = down_cols.reshape(-1, down_blocks.shape[2])
    flat_rows = lax.all_gather(arrived_cols, "head", axis=1, tiled=True)
    projected = jnp.einsum("rd,gfd->rgf", flat_rows, gate_up, preferred_element_type=jnp.float32)
    hidden = (jax.nn.silu(projected[:, 0]) * projected[:, 1]).astype(jnp.bfloat16)
    hidden_all = lax.all_gather(hidden, "head", axis=1, tiled=True)
    summed_cols = jnp.dot(hidden_all, down_cols, preferred_element_type=jnp.float32).astype(jnp.bfloat16)
    summed_rows = summed_cols.reshape(expert_count, capacity, -1)
    returned = lax.all_to_all(summed_rows, EXPERT, split_axis=0, concat_axis=0, tiled=True)
    back_rows = returned.reshape(expert_count * capacity, -1).astype(jnp.float32)
    mixture = jnp.dot(blending.T, back_rows, precision=lax.Precision.HIGHEST)
    return stream_cols + mixture


def solution(mesh):
    placed = (
        P(EXPERT, "head", None),
        P(EXPERT, "head", None),
        P(EXPERT, None, None),
        P(EXPERT, None, None),
        P(EXPERT),
        P("head", EXPERT),
        P(EXPERT, None),
        P(),
        P(EXPERT, None),
        P(EXPERT, None),
        P(EXPERT, None, "head", None),
        P(EXPERT, "head", None),
    )
    head_count, expert_total = mesh.devices.shape
    y_count = len({device.coords[1] for device in mesh.devices[0]})
    split_mesh = Mesh(
        mesh.devices.reshape(head_count, expert_total // y_count, y_count), ("head",) + EXPERT
    )
    return jax.shard_map(
        on_device, mesh=split_mesh, in_specs=placed, out_specs=P(EXPERT, "head"), check_vma=False
    )
```

```python
import jax
import jax.numpy as jnp
from jax import lax
from jax.sharding import Mesh
from jax.sharding import PartitionSpec as P

EXPERT = ("ez", "ey")
softmax_scale = 192.0 ** (-0.5)
norm_epsilon = 1e-06


def attend(q_latent, q_rotary, cache_latent, cache_rotary, lengths):
    scores = jnp.einsum("shl,scl->shc", q_latent, cache_latent, preferred_element_type=jnp.float32)
    scores = scores + jnp.einsum(
        "shr,src->shc", q_rotary, cache_rotary, preferred_element_type=jnp.float32
    )
    scores = scores * softmax_scale
    position = lax.broadcasted_iota(jnp.int32, scores.shape, 2)
    scores = jnp.where(position < lengths[:, None, None], scores, -1e30)
    highest = jnp.max(scores, axis=2, keepdims=True)
    weights = jnp.exp(scores - highest)
    probs = (weights / jnp.sum(weights, axis=2, keepdims=True)).astype(jnp.bfloat16)
    return jnp.einsum(
        "shc,scl->shl", probs, cache_latent, preferred_element_type=jnp.float32
    ).astype(jnp.bfloat16)


def on_device(
    q_latent,
    q_rotary,
    cache_latent,
    cache_rotary,
    lengths,
    w_value_out,
    resid,
    norm_gain,
    route_ids,
    route_weights,
    w_gate_up,
    w_down,
):
    seq_local = q_latent.shape[0]
    latent_out = attend(q_latent, q_rotary, cache_latent, cache_rotary, lengths)
    flattened = latent_out.reshape(seq_local, -1)
    z_count = lax.axis_size("ez")
    latent_copies = jnp.broadcast_to(flattened[None], (z_count,) + flattened.shape)
    gathered = lax.all_to_all(latent_copies, "ez", split_axis=0, concat_axis=0, tiled=True)
    gathered = gathered.reshape(-1, flattened.shape[1])
    value_blocks = lax.all_gather(w_value_out, "ey", axis=0, tiled=False)
    column_terms = jnp.einsum(
        "sk,jkc->sjc", gathered, value_blocks, preferred_element_type=jnp.float32
    ).reshape(gathered.shape[0], -1)
    column_sums = lax.psum(column_terms.astype(jnp.bfloat16), "head")
    attention = lax.all_to_all(
        column_sums, "ez", split_axis=0, concat_axis=1, tiled=True
    )
    stream = resid.astype(jnp.float32) + attention.astype(jnp.float32)
    mean_square = jnp.mean(stream * stream, axis=1, keepdims=True)
    normed = (stream * lax.rsqrt(mean_square + norm_epsilon) * norm_gain).astype(jnp.bfloat16)
    expert_count = lax.axis_size("ez") * lax.axis_size("ey")
    top_count = route_ids.shape[1]
    capacity = max(2, -(-(seq_local * top_count) // expert_count))
    flat_ids = route_ids.reshape(-1)
    one_hot = (flat_ids[:, None] == jnp.arange(expert_count, dtype=jnp.int32)[None, :]).astype(
        jnp.int32
    )
    earlier = jnp.cumsum(one_hot, axis=0) - one_hot
    slot_index = jnp.sum(earlier * one_hot, axis=1)
    target = (flat_ids * capacity + slot_index).reshape(seq_local, top_count)
    places = jnp.arange(expert_count * capacity, dtype=jnp.int32)
    matches = target[None, :, :] == places[:, None, None]
    selector = jnp.sum(matches.astype(jnp.int32), axis=2).astype(jnp.bfloat16)
    blending = jnp.sum(jnp.where(matches, route_weights[None, :, :], 0.0), axis=2)
    gate_up = w_gate_up[0]
    col_width = stream.shape[1] // lax.axis_size("head")
    offset = lax.axis_index("head") * col_width
    normed_cols = lax.dynamic_slice_in_dim(normed, offset, col_width, 1)
    outgoing = jnp.dot(selector, normed_cols, preferred_element_type=jnp.float32).astype(jnp.bfloat16)
    outgoing = outgoing.reshape(expert_count, capacity, -1)
    arrived = lax.all_to_all(outgoing, EXPERT, split_axis=0, concat_axis=0, tiled=True)
    arrived_cols = arrived.reshape(-1, arrived.shape[2])
    head_count = lax.axis_size("head")
    down_blocks = w_down[0].reshape(w_down.shape[1], head_count, -1)
    arrived_cols, down_blocks = lax.optimization_barrier((arrived_cols, down_blocks))
    down_cols = lax.all_to_all(down_blocks, "head", split_axis=1, concat_axis=0, tiled=True)
    down_cols = down_cols.reshape(-1, down_blocks.shape[2])
    flat_rows = lax.all_gather(arrived_cols, "head", axis=1, tiled=True)
    projected = jnp.einsum("rd,gfd->rgf", flat_rows, gate_up, preferred_element_type=jnp.float32)
    hidden = (jax.nn.silu(projected[:, 0]) * projected[:, 1]).astype(jnp.bfloat16)
    hidden_all = lax.all_gather(hidden, "head", axis=1, tiled=True)
    summed_cols = jnp.dot(hidden_all, down_cols, preferred_element_type=jnp.float32).astype(jnp.bfloat16)
    summed_rows = summed_cols.reshape(expert_count, capacity, -1)
    returned = lax.all_to_all(summed_rows, EXPERT, split_axis=0, concat_axis=0, tiled=True)
    back_rows = returned.reshape(expert_count * capacity, -1).astype(jnp.float32)
    mixture = jnp.dot(blending.T, back_rows, precision=lax.Precision.HIGHEST)
    stream_cols = lax.dynamic_slice_in_dim(stream, offset, col_width, 1)
    return stream_cols + mixture


def solution(mesh):
    placed = (
        P(EXPERT, "head", None),
        P(EXPERT, "head", None),
        P(EXPERT, None, None),
        P(EXPERT, None, None),
        P(EXPERT),
        P("head", EXPERT),
        P(EXPERT, None),
        P(),
        P(EXPERT, None),
        P(EXPERT, None),
        P(EXPERT, None, "head", None),
        P(EXPERT, "head", None),
    )
    head_count, expert_total = mesh.devices.shape
    y_count = len({device.coords[1] for device in mesh.devices[0]})
    split_mesh = Mesh(
        mesh.devices.reshape(head_count, expert_total // y_count, y_count), ("head",) + EXPERT
    )
    return jax.shard_map(
        on_device, mesh=split_mesh, in_specs=placed, out_specs=P(EXPERT, "head"), check_vma=False
    )
```

```python
import jax
import jax.numpy as jnp
from jax import lax
from jax.sharding import Mesh
from jax.sharding import PartitionSpec as P

EXPERT = ("ez", "ey")
softmax_scale = 192.0 ** (-0.5)
norm_epsilon = 1e-06


def attend(q_latent, q_rotary, cache_latent, cache_rotary, lengths):
    scores = jnp.einsum("shl,scl->shc", q_latent, cache_latent, preferred_element_type=jnp.float32)
    scores = scores + jnp.einsum(
        "shr,src->shc", q_rotary, cache_rotary, preferred_element_type=jnp.float32
    )
    scores = scores * softmax_scale
    position = lax.broadcasted_iota(jnp.int32, scores.shape, 2)
    scores = jnp.where(position < lengths[:, None, None], scores, -1e30)
    highest = jnp.max(scores, axis=2, keepdims=True)
    weights = jnp.exp(scores - highest)
    probs = (weights / jnp.sum(weights, axis=2, keepdims=True)).astype(jnp.bfloat16)
    return jnp.einsum(
        "shc,scl->shl", probs, cache_latent, preferred_element_type=jnp.float32
    ).astype(jnp.bfloat16)


def on_device(
    q_latent,
    q_rotary,
    cache_latent,
    cache_rotary,
    lengths,
    w_value_out,
    resid,
    norm_gain,
    route_ids,
    route_weights,
    w_gate_up,
    w_down,
):
    seq_local = q_latent.shape[0]
    latent_out = attend(q_latent, q_rotary, cache_latent, cache_rotary, lengths)
    flattened = latent_out.reshape(seq_local, -1)
    z_count = lax.axis_size("ez")
    latent_copies = jnp.broadcast_to(flattened[None], (z_count,) + flattened.shape)
    gathered = lax.all_to_all(latent_copies, "ez", split_axis=0, concat_axis=0, tiled=True)
    gathered = gathered.reshape(-1, flattened.shape[1])
    value_blocks = lax.all_gather(w_value_out, "ey", axis=0, tiled=False)
    column_terms = jnp.einsum(
        "sk,jkc->sjc", gathered, value_blocks, preferred_element_type=jnp.float32
    ).reshape(gathered.shape[0], -1)
    column_sums = lax.psum(column_terms, "head")
    attention = lax.all_to_all(
        column_sums.astype(jnp.bfloat16), "ez", split_axis=0, concat_axis=1, tiled=True
    )
    stream = resid.astype(jnp.float32) + attention.astype(jnp.float32)
    mean_square = jnp.mean(stream * stream, axis=1, keepdims=True)
    normed = (stream * lax.rsqrt(mean_square + norm_epsilon) * norm_gain).astype(jnp.bfloat16)
    expert_count = lax.axis_size("ez") * lax.axis_size("ey")
    top_count = route_ids.shape[1]
    capacity = max(2, -(-(seq_local * top_count) // expert_count))
    flat_ids = route_ids.reshape(-1)
    one_hot = (flat_ids[:, None] == jnp.arange(expert_count, dtype=jnp.int32)[None, :]).astype(
        jnp.int32
    )
    earlier = jnp.cumsum(one_hot, axis=0) - one_hot
    slot_index = jnp.sum(earlier * one_hot, axis=1)
    target = (flat_ids * capacity + slot_index).reshape(seq_local, top_count)
    places = jnp.arange(expert_count * capacity, dtype=jnp.int32)
    matches = target[None, :, :] == places[:, None, None]
    selector = jnp.sum(matches.astype(jnp.int32), axis=2).astype(jnp.bfloat16)
    blending = jnp.sum(jnp.where(matches, route_weights[None, :, :], 0.0), axis=2)
    gate_up = w_gate_up[0]
    col_width = stream.shape[1] // lax.axis_size("head")
    offset = lax.axis_index("head") * col_width
    normed_cols = lax.dynamic_slice_in_dim(normed, offset, col_width, 1)
    outgoing = jnp.dot(selector, normed_cols, preferred_element_type=jnp.float32).astype(jnp.bfloat16)
    outgoing = outgoing.reshape(expert_count, -1)
    arrived = lax.all_to_all(outgoing, EXPERT, split_axis=0, concat_axis=0, tiled=True)
    arrived_cols = arrived.reshape(expert_count * capacity, -1)
    head_count = lax.axis_size("head")
    down_blocks = w_down[0].reshape(w_down.shape[1], head_count, -1)
    arrived_cols, down_blocks = lax.optimization_barrier((arrived_cols, down_blocks))
    down_cols = lax.all_to_all(down_blocks, "head", split_axis=1, concat_axis=0, tiled=True)
    down_cols = down_cols.reshape(-1, down_blocks.shape[2])
    flat_rows = lax.all_gather(arrived_cols, "head", axis=1, tiled=True)
    projected = jnp.einsum("rd,gfd->rgf", flat_rows, gate_up, preferred_element_type=jnp.float32)
    hidden = (jax.nn.silu(projected[:, 0]) * projected[:, 1]).astype(jnp.bfloat16)
    hidden_all = lax.all_gather(hidden, "head", axis=1, tiled=True)
    summed_cols = jnp.dot(hidden_all, down_cols, preferred_element_type=jnp.float32).astype(jnp.bfloat16)
    summed_rows = summed_cols.reshape(expert_count, -1)
    returned = lax.all_to_all(summed_rows, EXPERT, split_axis=0, concat_axis=0, tiled=True)
    back_rows = returned.reshape(expert_count * capacity, -1).astype(jnp.float32)
    mixture = jnp.dot(blending.T, back_rows, precision=lax.Precision.HIGHEST)
    stream_cols = lax.dynamic_slice_in_dim(stream, offset, col_width, 1)
    return stream_cols + mixture


def solution(mesh):
    placed = (
        P(EXPERT, "head", None),
        P(EXPERT, "head", None),
        P(EXPERT, None, None),
        P(EXPERT, None, None),
        P(EXPERT),
        P("head", EXPERT),
        P(EXPERT, None),
        P(),
        P(EXPERT, None),
        P(EXPERT, None),
        P(EXPERT, None, "head", None),
        P(EXPERT, "head", None),
    )
    head_count, expert_total = mesh.devices.shape
    y_count = len({device.coords[1] for device in mesh.devices[0]})
    split_mesh = Mesh(
        mesh.devices.reshape(head_count, expert_total // y_count, y_count), ("head",) + EXPERT
    )
    return jax.shard_map(
        on_device, mesh=split_mesh, in_specs=placed, out_specs=P(EXPERT, "head"), check_vma=False
    )
```
